768 devices in a mesh: dp: 24 (over x_hi, z), row: 2 (over x_lo), fsdp: 16 (over y, core).
Axes of the slice: x: 4 (x_hi: 2, x_lo: 2; x = x_hi * 2 + x_lo), y: 8, z: 12, core: 2. Of those that a mesh axis runs over, the one named last changes fastest.
Arguments:
- images: bfloat16 [384, 16, 16, 1536], P(('dp', 'fsdp'), 'row'), may hold values from -6 to 6
- kernel: float32 [7, 7, 1536], replicated, may hold values from -0.875 to 0.875
- conv_bias: float32 [1536], replicated, may hold values from -3 to 3
- ln_gain: float32 [1536], replicated, may hold values from 0.5 to 2
- ln_shift: float32 [1536], replicated, may hold values from -3 to 3
- w_up: bfloat16 [1536, 3072], P('fsdp', 'row'), may hold values from -0.15625 to 0.15625
- cotangent: bfloat16 [384, 16, 16, 3072], P(('dp', 'fsdp'), None, None, 'row'), may hold values from -0.1875 to 0.1875
Outputs:
- hidden: bfloat16 [384, 16, 16, 3072], P(('dp', 'fsdp'), None, None, 'row')
- grad_weight: float32 [24, 1536, 3072], P('dp', 'fsdp', 'row')
- grad_kernel: float32 [7, 7, 1536], replicated
- grad_vectors: float32 [3, 1536], replicated
The draws below stay inside these ranges and needn't reach their ends.
All inputs are finite; a program needn't handle non-finite values.
Results may differ from the reference program's by a relative error of at most 0.02.
Values may be sent and summed in bfloat16 or wider, within the bound.
No kernel may reach another device: no remote copies, remote signals or barrier semaphores. Data moves between devices by JAX's collectives and lax.ppermute only.
A program may use at most 64 MiB of HBM per device.

```python
import math
import jax
import jax.numpy as jnp
from jax import lax

D = 1536
FF = 3072
KS = 7
MAP = 16
IMG_DEV = 1
IMAGES = 384
N_DP = 24
N_FSDP = 16


def block_scale(stream_key, dims, split, low, largest):
    gain = 1.0
    for position, parts in split:
        steps = jax.random.uniform(jax.random.fold_in(jax.random.fold_in(stream_key, 6), position), (parts,), jnp.float32, low / len(split), largest / len(split))
        gain = gain * jnp.repeat(jnp.exp(steps), dims[position] // parts).reshape((-1,) + (1,) * (len(dims) - 1 - position))
    return gain


def scatter_about(rng, shape, width, bound, split=(), held_as=jnp.bfloat16):
    level = block_scale(rng, shape, split, -0.22, 0.18) if split else 1.0
    result = jax.random.normal(rng, shape, jnp.float32) * width * level
    return jnp.minimum(jnp.maximum(result, -bound), bound).astype(held_as)


def setup_inputs(seed: int = 0) -> dict:
    seeds = jax.random.split(jax.random.key(seed), 8)
    images = scatter_about(seeds[0], (IMAGES, MAP, MAP, D), 1.0, 6.0, ((0, 384), (1, 2)))
    kernel = scatter_about(seeds[1], (KS, KS, D), (KS * KS) ** -0.5, 0.875, (), jnp.float32)
    conv_bias = scatter_about(seeds[2], (D,), 0.5, 3.0, (), jnp.float32)
    ln_gain = jnp.clip(jnp.exp(jax.random.uniform(seeds[3], (D,), jnp.float32, math.log(0.5), math.log(2.0))), 0.5, 2.0)
    ln_shift = scatter_about(seeds[4], (D,), 0.5, 3.0, (), jnp.float32)
    w_up = scatter_about(seeds[5], (D, FF), D ** -0.5, 0.15625, ((0, 16), (1, 2)))
    cotangent = scatter_about(seeds[6], (IMAGES, MAP, MAP, FF), (2.0 / (IMG_DEV * MAP * MAP * N_FSDP) ** 0.5), 0.1875, ((0, 384), (3, 2)))
    return dict(images=images, kernel=kernel, conv_bias=conv_bias, ln_gain=ln_gain, ln_shift=ln_shift, w_up=w_up, cotangent=cotangent)


norm_epsilon = 1e-06

def gelu_exact(values):
    return jax.nn.gelu(values, approximate=False)

def conv_norm(images, kernel, conv_bias, ln_gain, ln_shift):
    source = images.astype(jnp.float32)
    map_side = source.shape[1]
    padded = jnp.pad(source, ((0, 0), (3, 3), (3, 3), (0, 0)))
    conv_out = jnp.zeros_like(source) + conv_bias
    for tap_row in range(7):
        for tap_col in range(7):
            conv_out = conv_out + padded[:, tap_row:tap_row + map_side, tap_col:tap_col + map_side, :] * kernel[tap_row, tap_col]
    centre = lax.optimization_barrier(jnp.mean(conv_out, axis=-1, keepdims=True))
    spread = lax.optimization_barrier(jnp.mean(jnp.square(conv_out - centre), axis=-1, keepdims=True))
    scale_inv = lax.rsqrt(spread + norm_epsilon)
    unit_field = (conv_out - centre) * scale_inv
    normed = (unit_field * ln_gain + ln_shift).astype(jnp.bfloat16)
    return (padded, unit_field, scale_inv, normed)

def norm_conv_grads(padded, unit_field, scale_inv, grad_normed, ln_gain):
    map_side = unit_field.shape[1]
    grad_gain = lax.optimization_barrier(jnp.sum(grad_normed * unit_field, axis=(0, 1, 2)))
    grad_shift = lax.optimization_barrier(jnp.sum(grad_normed, axis=(0, 1, 2)))
    grad_unit = grad_normed * ln_gain
    mean_one = lax.optimization_barrier(jnp.mean(grad_unit, axis=-1, keepdims=True))
    mean_two = lax.optimization_barrier(jnp.mean(grad_unit * unit_field, axis=-1, keepdims=True))
    grad_conv = scale_inv * (grad_unit - mean_one - unit_field * mean_two)
    grad_bias = lax.optimization_barrier(jnp.sum(grad_conv, axis=(0, 1, 2)))
    tap_sums = []
    for tap_row in range(7):
        for tap_col in range(7):
            window = padded[:, tap_row:tap_row + map_side, tap_col:tap_col + map_side, :]
            tap_sums.append(lax.optimization_barrier(jnp.sum(window * grad_conv, axis=(0, 1, 2))))
    grad_kernel = jnp.stack(tap_sums).reshape(7, 7, unit_field.shape[-1])
    return (grad_kernel, jnp.stack([grad_bias, grad_gain, grad_shift]))

def reference(images, kernel, conv_bias, ln_gain, ln_shift, w_up, cotangent):
    map_side = images.shape[1]
    blocks = images.reshape(N_DP, N_FSDP, IMG_DEV, map_side, map_side, D)
    cot_blocks = cotangent.reshape(N_DP, N_FSDP, IMG_DEV, map_side, map_side, FF)

    def one_device(state_pair, inputs_pair):
        weight_sum, kernel_sum, vector_sum = state_pair
        group_images, group_cot = inputs_pair
        padded, unit_field, scale_inv, normed = conv_norm(group_images, kernel, conv_bias, ln_gain, ln_shift)
        flat = normed.reshape(-1, D)
        pre_act = jnp.dot(flat, w_up, preferred_element_type=jnp.float32)
        activated, pullback = jax.vjp(gelu_exact, pre_act)
        hidden = activated.astype(jnp.bfloat16)
        grad_pre = pullback(group_cot.reshape(-1, FF).astype(jnp.float32))[0].astype(jnp.bfloat16)
        weight_term = lax.dot_general(flat, grad_pre, (((0,), (0,)), ((), ())), preferred_element_type=jnp.float32)
        rounded = lax.optimization_barrier(weight_term.astype(jnp.bfloat16))
        weight_sum = weight_sum + rounded.astype(jnp.float32)
        grad_normed = lax.dot_general(grad_pre, w_up, (((1,), (1,)), ((), ())), preferred_element_type=jnp.float32)
        grad_kernel, grad_vectors = norm_conv_grads(padded, unit_field, scale_inv, grad_normed.reshape(unit_field.shape), ln_gain)
        new_state = (weight_sum, kernel_sum + grad_kernel, vector_sum + grad_vectors)
        return (new_state, hidden.reshape(IMG_DEV, map_side, map_side, FF))

    def one_replica(inputs_pair):
        initial = (jnp.zeros((D, FF), jnp.float32), jnp.zeros((7, 7, D), jnp.float32), jnp.zeros((3, D), jnp.float32))
        final_state, hidden = lax.scan(one_device, initial, inputs_pair)
        return (final_state[0], final_state[1], final_state[2], hidden)
    weight_sums, kernel_sums, vector_sums, hiddens = lax.map(one_replica, (blocks, cot_blocks))
    hidden_all = hiddens.reshape(N_DP * N_FSDP * IMG_DEV, map_side, map_side, FF)
    return (hidden_all, weight_sums, lax.optimization_barrier(jnp.sum(kernel_sums, axis=0)), lax.optimization_barrier(jnp.sum(vector_sums, axis=0)))
```

```python
import jax
import jax.numpy as jnp
from jax import lax
from jax.sharding import PartitionSpec as P

norm_epsilon = 1e-06


def gelu_exact(values):
    return jax.nn.gelu(values, approximate=False)


def conv_norm(images, kernel, conv_bias, ln_gain, ln_shift):
    source = images.astype(jnp.float32)
    map_side = source.shape[1]
    padded = jnp.pad(source, ((0, 0), (3, 3), (3, 3), (0, 0)))
    conv_out = jnp.zeros_like(source) + conv_bias
    for tap_row in range(7):
        for tap_col in range(7):
            conv_out = (
                conv_out
                + padded[:, tap_row : tap_row + map_side, tap_col : tap_col + map_side, :]
                * kernel[tap_row, tap_col]
            )
    centre = jnp.mean(conv_out, axis=-1, keepdims=True)
    spread = jnp.mean(jnp.square(conv_out - centre), axis=-1, keepdims=True)
    scale_inv = lax.rsqrt(spread + norm_epsilon)
    unit_field = (conv_out - centre) * scale_inv
    normed = (unit_field * ln_gain + ln_shift).astype(jnp.bfloat16)
    return (padded, unit_field, scale_inv, normed)


def norm_conv_grads(padded, unit_field, scale_inv, grad_normed, ln_gain):
    map_side = unit_field.shape[1]
    grad_gain = jnp.sum(grad_normed * unit_field, axis=(0, 1, 2))
    grad_shift = jnp.sum(grad_normed, axis=(0, 1, 2))
    grad_unit = grad_normed * ln_gain
    mean_one = jnp.mean(grad_unit, axis=-1, keepdims=True)
    mean_two = jnp.mean(grad_unit * unit_field, axis=-1, keepdims=True)
    grad_conv = scale_inv * (grad_unit - mean_one - unit_field * mean_two)
    grad_bias = jnp.sum(grad_conv, axis=(0, 1, 2))
    tap_sums = []
    for tap_row in range(7):
        for tap_col in range(7):
            window = padded[:, tap_row : tap_row + map_side, tap_col : tap_col + map_side, :]
            tap_sums.append(jnp.sum(window * grad_conv, axis=(0, 1, 2)))
    grad_kernel = jnp.stack(tap_sums).reshape(7, 7, unit_field.shape[-1])
    return (grad_kernel, jnp.stack([grad_bias, grad_gain, grad_shift]))


def tree_sum(values, axis):
    size = lax.axis_size(axis)
    span = 1
    while size % (2 * span) == 0:
        partners = [(i, i ^ span) for i in range(size)]
        values = values + lax.ppermute(values, axis, partners)
        span *= 2
    groups = size // span
    if groups == 1:
        return values
    received = [values]
    for shift in range(1, groups):
        pairs = [(i, (i + shift * span) % size) for i in range(size)]
        received.append(lax.ppermute(values, axis, pairs))
    group = lax.axis_index(axis) // span
    stacked = jnp.stack(received)
    total = None
    for source in range(groups):
        term = stacked[(group - source) % groups]
        total = term if total is None else total + term
    return total


def shards(images, kernel, conv_bias, ln_gain, ln_shift, w_up, cotangent):
    full_maps = lax.all_gather(images, "row", axis=1, tiled=True)
    padded, unit_field, scale_inv, normed = conv_norm(
        full_maps, kernel, conv_bias, ln_gain, ln_shift
    )
    channels = normed.shape[-1]
    hidden_units = w_up.shape[1]
    flat = normed.reshape(-1, channels)
    weights = lax.all_gather(w_up, "fsdp", axis=0, tiled=True)
    pre_act = jnp.dot(flat, weights, preferred_element_type=jnp.float32)
    activated, pullback = jax.vjp(gelu_exact, pre_act)
    hidden = activated.astype(jnp.bfloat16)
    grad_pre = pullback(cotangent.reshape(-1, hidden_units).astype(jnp.float32))[0].astype(
        jnp.bfloat16
    )
    grad_weight = lax.psum_scatter(
        lax.dot_general(
            flat, grad_pre, (((0,), (0,)), ((), ())), preferred_element_type=jnp.float32
        ).astype(jnp.bfloat16),
        "fsdp",
        scatter_dimension=0,
        tiled=True,
    ).astype(jnp.float32)
    grad_normed = lax.dot_general(
        grad_pre, weights, (((1,), (1,)), ((), ())), preferred_element_type=jnp.float32
    )
    kernel_part, vector_part = norm_conv_grads(
        padded, unit_field, scale_inv, grad_normed.reshape(unit_field.shape), ln_gain
    )
    taps = kernel_part.shape[0] * kernel_part.shape[1]
    packed = jnp.concatenate([kernel_part.reshape(taps, channels), vector_part], axis=0)
    packed = tree_sum(tree_sum(tree_sum(packed, "row"), "fsdp"), "dp")
    grad_kernel = packed[:taps].reshape(kernel_part.shape)
    grad_vectors = packed[taps:]
    return (hidden.reshape(cotangent.shape), grad_weight[None], grad_kernel, grad_vectors)


def solution(mesh):
    return jax.shard_map(
        shards,
        mesh=mesh,
        in_specs=(
            P(("dp", "fsdp"), "row", None, None),
            P(),
            P(),
            P(),
            P(),
            P("fsdp", "row"),
            P(("dp", "fsdp"), None, None, "row"),
        ),
        out_specs=(P(("dp", "fsdp"), None, None, "row"), P("dp", "fsdp", "row"), P(), P()),
        check_vma=False,
    )
```

```python
import jax
import jax.numpy as jnp
from jax import lax
from jax.sharding import PartitionSpec as P

norm_epsilon = 1e-06


def gelu_exact(values):
    return jax.nn.gelu(values, approximate=False)


def conv_norm(images, kernel, conv_bias, ln_gain, ln_shift):
    source = images.astype(jnp.float32)
    map_side = source.shape[1]
    padded = jnp.pad(source, ((0, 0), (3, 3), (3, 3), (0, 0)))
    conv_out = jnp.zeros_like(source) + conv_bias
    for tap_row in range(7):
        for tap_col in range(7):
            conv_out = (
                conv_out
                + padded[:, tap_row : tap_row + map_side, tap_col : tap_col + map_side, :]
                * kernel[tap_row, tap_col]
            )
    centre = jnp.mean(conv_out, axis=-1, keepdims=True)
    spread = jnp.mean(jnp.square(conv_out - centre), axis=-1, keepdims=True)
    scale_inv = lax.rsqrt(spread + norm_epsilon)
    unit_field = (conv_out - centre) * scale_inv
    normed = (unit_field * ln_gain + ln_shift).astype(jnp.bfloat16)
    return (padded, unit_field, scale_inv, normed)


def norm_conv_grads(padded, unit_field, scale_inv, grad_normed, ln_gain):
    map_side = unit_field.shape[1]
    grad_gain = jnp.sum(grad_normed * unit_field, axis=(0, 1, 2))
    grad_shift = jnp.sum(grad_normed, axis=(0, 1, 2))
    grad_unit = grad_normed * ln_gain
    mean_one = jnp.mean(grad_unit, axis=-1, keepdims=True)
    mean_two = jnp.mean(grad_unit * unit_field, axis=-1, keepdims=True)
    grad_conv = scale_inv * (grad_unit - mean_one - unit_field * mean_two)
    grad_bias = jnp.sum(grad_conv, axis=(0, 1, 2))
    tap_sums = []
    for tap_row in range(7):
        for tap_col in range(7):
            window = padded[:, tap_row : tap_row + map_side, tap_col : tap_col + map_side, :]
            tap_sums.append(jnp.sum(window * grad_conv, axis=(0, 1, 2)))
    grad_kernel = jnp.stack(tap_sums).reshape(7, 7, unit_field.shape[-1])
    return (grad_kernel, jnp.stack([grad_bias, grad_gain, grad_shift]))


def halving_sum(values, stages):
    kept = []
    for axis, span in stages:
        size = lax.axis_size(axis)
        bit = (lax.axis_index(axis) // span) % 2
        half = values.shape[0] // 2
        keep = lax.dynamic_slice_in_dim(values, bit * half, half)
        send = lax.dynamic_slice_in_dim(values, (1 - bit) * half, half)
        values = keep + lax.ppermute(send, axis, [(i, i ^ span) for i in range(size)])
        kept.append((axis, span, size, bit))
    axis, span = "dp", 1
    while lax.axis_size(axis) % (2 * span) == 0 and ("dp", span) in stages:
        span *= 2
    size = lax.axis_size(axis)
    groups = size // span
    if groups > 1:
        group = lax.axis_index(axis) // span
        parts = values.reshape(groups, -1)
        received = [parts[group]]
        for shift in range(1, groups):
            pairs = [(i, (i + shift * span) % size) for i in range(size)]
            received.append(lax.ppermute(parts[(group + shift) % groups], axis, pairs))
        stacked = jnp.stack(received)
        total = None
        for source in range(groups):
            term = stacked[(group - source) % groups]
            total = term if total is None else total + term
        received = [total]
        for shift in range(1, groups):
            pairs = [(i, (i + shift * span) % size) for i in range(size)]
            received.append(lax.ppermute(total, axis, pairs))
        stacked = jnp.stack(received)
        values = jnp.concatenate([stacked[(group - source) % groups] for source in range(groups)])
    for axis, span, size, bit in reversed(kept):
        other = lax.ppermute(values, axis, [(i, i ^ span) for i in range(size)])
        values = jnp.where(bit == 0, jnp.concatenate([values, other]), jnp.concatenate([other, values]))
    return values


HALVING_STAGES = (
    ("fsdp", 1), ("row", 1), ("fsdp", 2), ("dp", 1), ("fsdp", 4), ("dp", 2), ("fsdp", 8), ("dp", 4),
)


def shards(images, kernel, conv_bias, ln_gain, ln_shift, w_up, cotangent):
    full_maps = lax.all_gather(images, "row", axis=1, tiled=True)
    padded, unit_field, scale_inv, normed = conv_norm(
        full_maps, kernel, conv_bias, ln_gain, ln_shift
    )
    channels = normed.shape[-1]
    hidden_units = w_up.shape[1]
    flat = normed.reshape(-1, channels)
    weights = lax.all_gather(w_up, "fsdp", axis=0, tiled=True)
    pre_act = jnp.dot(flat, weights, preferred_element_type=jnp.float32)
    activated, pullback = jax.vjp(gelu_exact, pre_act)
    hidden = activated.astype(jnp.bfloat16)
    grad_pre = pullback(cotangent.reshape(-1, hidden_units).astype(jnp.float32))[0].astype(
        jnp.bfloat16
    )
    grad_weight = lax.psum_scatter(
        lax.dot_general(
            flat, grad_pre, (((0,), (0,)), ((), ())), preferred_element_type=jnp.float32
        ).astype(jnp.bfloat16),
        "fsdp",
        scatter_dimension=0,
        tiled=True,
    ).astype(jnp.float32)
    grad_normed = lax.dot_general(
        grad_pre, weights, (((1,), (1,)), ((), ())), preferred_element_type=jnp.float32
    )
    kernel_part, vector_part = norm_conv_grads(
        padded, unit_field, scale_inv, grad_normed.reshape(unit_field.shape), ln_gain
    )
    taps = kernel_part.shape[0] * kernel_part.shape[1]
    packed = jnp.concatenate([kernel_part.reshape(taps, channels), vector_part], axis=0)
    packed = halving_sum(packed.reshape(-1), HALVING_STAGES).reshape(packed.shape)
    grad_kernel = packed[:taps].reshape(kernel_part.shape)
    grad_vectors = packed[taps:]
    return (hidden.reshape(cotangent.shape), grad_weight[None], grad_kernel, grad_vectors)


def solution(mesh):
    return jax.shard_map(
        shards,
        mesh=mesh,
        in_specs=(
            P(("dp", "fsdp"), "row", None, None),
            P(),
            P(),
            P(),
            P(),
            P("fsdp", "row"),
            P(("dp", "fsdp"), None, None, "row"),
        ),
        out_specs=(P(("dp", "fsdp"), None, None, "row"), P("dp", "fsdp", "row"), P(), P()),
        check_vma=False,
    )
```

```python
import jax
import jax.numpy as jnp
from jax import lax
from jax.sharding import PartitionSpec as P

norm_epsilon = 1e-06


def gelu_exact(values):
    return jax.nn.gelu(values, approximate=False)


def conv_norm(images, kernel, conv_bias, ln_gain, ln_shift):
    source = images.astype(jnp.float32)
    map_side = source.shape[1]
    padded = jnp.pad(source, ((0, 0), (3, 3), (3, 3), (0, 0)))
    conv_out = jnp.zeros_like(source) + conv_bias
    for tap_row in range(7):
        for tap_col in range(7):
            conv_out = (
                conv_out
                + padded[:, tap_row : tap_row + map_side, tap_col : tap_col + map_side, :]
                * kernel[tap_row, tap_col]
            )
    centre = jnp.mean(conv_out, axis=-1, keepdims=True)
    spread = jnp.mean(jnp.square(conv_out - centre), axis=-1, keepdims=True)
    scale_inv = lax.rsqrt(spread + norm_epsilon)
    unit_field = (conv_out - centre) * scale_inv
    normed = (unit_field * ln_gain + ln_shift).astype(jnp.bfloat16)
    return (padded, unit_field, scale_inv, normed)


def norm_conv_grads(padded, unit_field, scale_inv, grad_normed, ln_gain):
    map_side = unit_field.shape[1]
    grad_gain = jnp.sum(grad_normed * unit_field, axis=(0, 1, 2))
    grad_shift = jnp.sum(grad_normed, axis=(0, 1, 2))
    grad_unit = grad_normed * ln_gain
    mean_one = jnp.mean(grad_unit, axis=-1, keepdims=True)
    mean_two = jnp.mean(grad_unit * unit_field, axis=-1, keepdims=True)
    grad_conv = scale_inv * (grad_unit - mean_one - unit_field * mean_two)
    grad_bias = jnp.sum(grad_conv, axis=(0, 1, 2))
    tap_sums = []
    for tap_row in range(7):
        for tap_col in range(7):
            window = padded[:, tap_row : tap_row + map_side, tap_col : tap_col + map_side, :]
            tap_sums.append(jnp.sum(window * grad_conv, axis=(0, 1, 2)))
    grad_kernel = jnp.stack(tap_sums).reshape(7, 7, unit_field.shape[-1])
    return (grad_kernel, jnp.stack([grad_bias, grad_gain, grad_shift]))


def exchange_sum(values, axes):
    count = lax.axis_size(axes)
    return lax.all_to_all(values.reshape(count, -1), axes, 0, 0, tiled=True).sum(0)


def exchange_gather(values, axes):
    count = lax.axis_size(axes)
    copies = jnp.broadcast_to(values[None], (count,) + values.shape)
    return lax.all_to_all(copies, axes, 0, 0, tiled=True).reshape(-1)


def packed_sum(values):
    inner, outer = ("row", "fsdp"), "dp"
    values = exchange_sum(exchange_sum(values, inner), outer)
    return exchange_gather(exchange_gather(values, outer), inner)


def shards(images, kernel, conv_bias, ln_gain, ln_shift, w_up, cotangent):
    full_maps = lax.all_gather(images, "row", axis=1, tiled=True)
    padded, unit_field, scale_inv, normed = conv_norm(
        full_maps, kernel, conv_bias, ln_gain, ln_shift
    )
    channels = normed.shape[-1]
    hidden_units = w_up.shape[1]
    flat = normed.reshape(-1, channels)
    weights = lax.all_gather(w_up, "fsdp", axis=0, tiled=True)
    pre_act = jnp.dot(flat, weights, preferred_element_type=jnp.float32)
    activated, pullback = jax.vjp(gelu_exact, pre_act)
    hidden = activated.astype(jnp.bfloat16)
    grad_pre = pullback(cotangent.reshape(-1, hidden_units).astype(jnp.float32))[0].astype(
        jnp.bfloat16
    )
    grad_weight = lax.psum_scatter(
        lax.dot_general(
            flat, grad_pre, (((0,), (0,)), ((), ())), preferred_element_type=jnp.float32
        ).astype(jnp.bfloat16),
        "fsdp",
        scatter_dimension=0,
        tiled=True,
    ).astype(jnp.float32)
    grad_normed = lax.dot_general(
        grad_pre, weights, (((1,), (1,)), ((), ())), preferred_element_type=jnp.float32
    )
    kernel_part, vector_part = norm_conv_grads(
        padded, unit_field, scale_inv, grad_normed.reshape(unit_field.shape), ln_gain
    )
    taps = kernel_part.shape[0] * kernel_part.shape[1]
    packed = jnp.concatenate([kernel_part.reshape(taps, channels), vector_part], axis=0)
    packed = packed_sum(packed.reshape(-1)).reshape(packed.shape)
    grad_kernel = packed[:taps].reshape(kernel_part.shape)
    grad_vectors = packed[taps:]
    return (hidden.reshape(cotangent.shape), grad_weight[None], grad_kernel, grad_vectors)


def solution(mesh):
    return jax.shard_map(
        shards,
        mesh=mesh,
        in_specs=(
            P(("dp", "fsdp"), "row", None, None),
            P(),
            P(),
            P(),
            P(),
            P("fsdp", "row"),
            P(("dp", "fsdp"), None, None, "row"),
        ),
        out_specs=(P(("dp", "fsdp"), None, None, "row"), P("dp", "fsdp", "row"), P(), P()),
        check_vma=False,
    )
```

```python
import jax
import jax.numpy as jnp
from jax import lax
from jax.sharding import PartitionSpec as P

norm_epsilon = 1e-06


def gelu_exact(values):
    return jax.nn.gelu(values, approximate=False)


def conv_norm(images, kernel, conv_bias, ln_gain, ln_shift):
    source = images.astype(jnp.float32)
    map_side = source.shape[1]
    padded = jnp.pad(source, ((0, 0), (3, 3), (3, 3), (0, 0)))
    conv_out = jnp.zeros_like(source) + conv_bias
    for tap_row in range(7):
        for tap_col in range(7):
            conv_out = (
                conv_out
                + padded[:, tap_row : tap_row + map_side, tap_col : tap_col + map_side, :]
                * kernel[tap_row, tap_col]
            )
    centre = jnp.mean(conv_out, axis=-1, keepdims=True)
    spread = jnp.mean(jnp.square(conv_out - centre), axis=-1, keepdims=True)
    scale_inv = lax.rsqrt(spread + norm_epsilon)
    unit_field = (conv_out - centre) * scale_inv
    normed = (unit_field * ln_gain + ln_shift).astype(jnp.bfloat16)
    return (padded, unit_field, scale_inv, normed)


def norm_conv_grads(padded, unit_field, scale_inv, grad_normed, ln_gain):
    map_side = unit_field.shape[1]
    grad_gain = jnp.sum(grad_normed * unit_field, axis=(0, 1, 2))
    grad_shift = jnp.sum(grad_normed, axis=(0, 1, 2))
    grad_unit = grad_normed * ln_gain
    mean_one = jnp.mean(grad_unit, axis=-1, keepdims=True)
    mean_two = jnp.mean(grad_unit * unit_field, axis=-1, keepdims=True)
    grad_conv = scale_inv * (grad_unit - mean_one - unit_field * mean_two)
    grad_bias = jnp.sum(grad_conv, axis=(0, 1, 2))
    tap_sums = []
    for tap_row in range(7):
        for tap_col in range(7):
            window = padded[:, tap_row : tap_row + map_side, tap_col : tap_col + map_side, :]
            tap_sums.append(jnp.sum(window * grad_conv, axis=(0, 1, 2)))
    grad_kernel = jnp.stack(tap_sums).reshape(7, 7, unit_field.shape[-1])
    return (grad_kernel, jnp.stack([grad_bias, grad_gain, grad_shift]))


def exchange_sum(values, axes):
    count = lax.axis_size(axes)
    return lax.all_to_all(values.reshape(count, -1), axes, 0, 0, tiled=True).sum(0)


def exchange_gather(values, axes):
    count = lax.axis_size(axes)
    copies = jnp.broadcast_to(values[None], (count,) + values.shape)
    return lax.all_to_all(copies, axes, 0, 0, tiled=True).reshape(-1)


def packed_sum(values):
    inner, outer = ("row", "fsdp"), "dp"
    values = exchange_sum(values, inner)
    values = exchange_gather(values, outer).reshape(lax.axis_size(outer), -1).sum(0)
    return exchange_gather(values, inner)


def shards(images, kernel, conv_bias, ln_gain, ln_shift, w_up, cotangent):
    full_maps = lax.all_gather(images, "row", axis=1, tiled=True)
    padded, unit_field, scale_inv, normed = conv_norm(
        full_maps, kernel, conv_bias, ln_gain, ln_shift
    )
    channels = normed.shape[-1]
    hidden_units = w_up.shape[1]
    flat = normed.reshape(-1, channels)
    weights = lax.all_gather(w_up, "fsdp", axis=0, tiled=True)
    pre_act = jnp.dot(flat, weights, preferred_element_type=jnp.float32)
    activated, pullback = jax.vjp(gelu_exact, pre_act)
    hidden = activated.astype(jnp.bfloat16)
    grad_pre = pullback(cotangent.reshape(-1, hidden_units).astype(jnp.float32))[0].astype(
        jnp.bfloat16
    )
    grad_weight = lax.psum_scatter(
        lax.dot_general(
            flat, grad_pre, (((0,), (0,)), ((), ())), preferred_element_type=jnp.float32
        ).astype(jnp.bfloat16),
        "fsdp",
        scatter_dimension=0,
        tiled=True,
    ).astype(jnp.float32)
    grad_normed = lax.dot_general(
        grad_pre, weights, (((1,), (1,)), ((), ())), preferred_element_type=jnp.float32
    )
    kernel_part, vector_part = norm_conv_grads(
        padded, unit_field, scale_inv, grad_normed.reshape(unit_field.shape), ln_gain
    )
    taps = kernel_part.shape[0] * kernel_part.shape[1]
    packed = jnp.concatenate([kernel_part.reshape(taps, channels), vector_part], axis=0)
    packed = packed_sum(packed.reshape(-1)).reshape(packed.shape)
    grad_kernel = packed[:taps].reshape(kernel_part.shape)
    grad_vectors = packed[taps:]
    return (hidden.reshape(cotangent.shape), grad_weight[None], grad_kernel, grad_vectors)


def solution(mesh):
    return jax.shard_map(
        shards,
        mesh=mesh,
        in_specs=(
            P(("dp", "fsdp"), "row", None, None),
            P(),
            P(),
            P(),
            P(),
            P("fsdp", "row"),
            P(("dp", "fsdp"), None, None, "row"),
        ),
        out_specs=(P(("dp", "fsdp"), None, None, "row"), P("dp", "fsdp", "row"), P(), P()),
        check_vma=False,
    )
```

```python
import jax
import jax.numpy as jnp
from jax import lax
from jax.sharding import PartitionSpec as P

norm_epsilon = 1e-06


def gelu_exact(values):
    return jax.nn.gelu(values, approximate=False)


def conv_norm(images, kernel, conv_bias, ln_gain, ln_shift):
    source = images.astype(jnp.float32)
    map_side = source.shape[1]
    padded = jnp.pad(source, ((0, 0), (3, 3), (3, 3), (0, 0)))
    conv_out = jnp.zeros_like(source) + conv_bias
    for tap_row in range(7):
        for tap_col in range(7):
            conv_out = (
                conv_out
                + padded[:, tap_row : tap_row + map_side, tap_col : tap_col + map_side, :]
                * kernel[tap_row, tap_col]
            )
    centre = jnp.mean(conv_out, axis=-1, keepdims=True)
    spread = jnp.mean(jnp.square(conv_out - centre), axis=-1, keepdims=True)
    scale_inv = lax.rsqrt(spread + norm_epsilon)
    unit_field = (conv_out - centre) * scale_inv
    normed = (unit_field * ln_gain + ln_shift).astype(jnp.bfloat16)
    return (padded, unit_field, scale_inv, normed)


def norm_conv_grads(padded, unit_field, scale_inv, grad_normed, ln_gain):
    map_side = unit_field.shape[1]
    grad_gain = jnp.sum(grad_normed * unit_field, axis=(0, 1, 2))
    grad_shift = jnp.sum(grad_normed, axis=(0, 1, 2))
    grad_unit = grad_normed * ln_gain
    mean_one = jnp.mean(grad_unit, axis=-1, keepdims=True)
    mean_two = jnp.mean(grad_unit * unit_field, axis=-1, keepdims=True)
    grad_conv = scale_inv * (grad_unit - mean_one - unit_field * mean_two)
    grad_bias = jnp.sum(grad_conv, axis=(0, 1, 2))
    tap_sums = []
    for tap_row in range(7):
        for tap_col in range(7):
            window = padded[:, tap_row : tap_row + map_side, tap_col : tap_col + map_side, :]
            tap_sums.append(jnp.sum(window * grad_conv, axis=(0, 1, 2)))
    grad_kernel = jnp.stack(tap_sums).reshape(7, 7, unit_field.shape[-1])
    return (grad_kernel, jnp.stack([grad_bias, grad_gain, grad_shift]))


def exchange_sum(values, axes):
    count = lax.axis_size(axes)
    return lax.all_to_all(values.reshape(count, -1), axes, 0, 0, tiled=True).sum(0)


def exchange_gather(values, axes):
    count = lax.axis_size(axes)
    copies = jnp.broadcast_to(values[None], (count,) + values.shape)
    return lax.all_to_all(copies, axes, 0, 0, tiled=True).reshape(-1)


def packed_sum(values):
    inner, outer = ("row", "fsdp"), "dp"
    values = exchange_sum(values, inner)
    values = exchange_gather(values, outer).reshape(lax.axis_size(outer), -1).sum(0)
    return exchange_gather(values, inner)


def shards(images, kernel, conv_bias, ln_gain, ln_shift, w_up, cotangent):
    full_maps = lax.all_gather(images, "row", axis=1, tiled=True)
    padded, unit_field, scale_inv, normed = conv_norm(
        full_maps, kernel, conv_bias, ln_gain, ln_shift
    )
    channels = normed.shape[-1]
    hidden_units = w_up.shape[1]
    flat = normed.reshape(-1, channels)
    cot_flat = cotangent.reshape(-1, hidden_units)
    pieces = 2
    width = hidden_units // pieces
    hidden_parts, weight_parts, grad_normed = [], [], None
    for piece in range(pieces):
        columns = slice(piece * width, (piece + 1) * width)
        weights = lax.all_gather(w_up[:, columns], "fsdp", axis=0, tiled=True)
        pre_act = jnp.dot(flat, weights, preferred_element_type=jnp.float32)
        activated, pullback = jax.vjp(gelu_exact, pre_act)
        hidden_parts.append(activated.astype(jnp.bfloat16))
        grad_pre = pullback(cot_flat[:, columns].astype(jnp.float32))[0].astype(jnp.bfloat16)
        weight_parts.append(
            lax.psum_scatter(
                lax.dot_general(
                    flat, grad_pre, (((0,), (0,)), ((), ())), preferred_element_type=jnp.float32
                ).astype(jnp.bfloat16),
                "fsdp",
                scatter_dimension=0,
                tiled=True,
            ).astype(jnp.float32)
        )
        part = lax.dot_general(
            grad_pre, weights, (((1,), (1,)), ((), ())), preferred_element_type=jnp.float32
        )
        grad_normed = part if grad_normed is None else grad_normed + part
    hidden = jnp.concatenate(hidden_parts, axis=1)
    grad_weight = jnp.concatenate(weight_parts, axis=1)
    kernel_part, vector_part = norm_conv_grads(
        padded, unit_field, scale_inv, grad_normed.reshape(unit_field.shape), ln_gain
    )
    taps = kernel_part.shape[0] * kernel_part.shape[1]
    packed = jnp.concatenate([kernel_part.reshape(taps, channels), vector_part], axis=0)
    packed = packed_sum(packed.reshape(-1)).reshape(packed.shape)
    grad_kernel = packed[:taps].reshape(kernel_part.shape)
    grad_vectors = packed[taps:]
    return (hidden.reshape(cotangent.shape), grad_weight[None], grad_kernel, grad_vectors)


def solution(mesh):
    return jax.shard_map(
        shards,
        mesh=mesh,
        in_specs=(
            P(("dp", "fsdp"), "row", None, None),
            P(),
            P(),
            P(),
            P(),
            P("fsdp", "row"),
            P(("dp", "fsdp"), None, None, "row"),
        ),
        out_specs=(P(("dp", "fsdp"), None, None, "row"), P("dp", "fsdp", "row"), P(), P()),
        check_vma=False,
    )
```

```python
import jax
import jax.numpy as jnp
from jax import lax
from jax.sharding import PartitionSpec as P

norm_epsilon = 1e-06


def gelu_exact(values):
    return jax.nn.gelu(values, approximate=False)


def conv_norm(images, kernel, conv_bias, ln_gain, ln_shift):
    source = images.astype(jnp.float32)
    map_side = source.shape[1]
    padded = jnp.pad(source, ((0, 0), (3, 3), (3, 3), (0, 0)))
    conv_out = jnp.zeros_like(source) + conv_bias
    for tap_row in range(7):
        for tap_col in range(7):
            conv_out = (
                conv_out
                + padded[:, tap_row : tap_row + map_side, tap_col : tap_col + map_side, :]
                * kernel[tap_row, tap_col]
            )
    centre = jnp.mean(conv_out, axis=-1, keepdims=True)
    spread = jnp.mean(jnp.square(conv_out - centre), axis=-1, keepdims=True)
    scale_inv = lax.rsqrt(spread + norm_epsilon)
    unit_field = (conv_out - centre) * scale_inv
    normed = (unit_field * ln_gain + ln_shift).astype(jnp.bfloat16)
    return (padded, unit_field, scale_inv, normed)


def norm_conv_grads(padded, unit_field, scale_inv, grad_normed, ln_gain):
    map_side = unit_field.shape[1]
    grad_gain = jnp.sum(grad_normed * unit_field, axis=(0, 1, 2))
    grad_shift = jnp.sum(grad_normed, axis=(0, 1, 2))
    grad_unit = grad_normed * ln_gain
    mean_one = jnp.mean(grad_unit, axis=-1, keepdims=True)
    mean_two = jnp.mean(grad_unit * unit_field, axis=-1, keepdims=True)
    grad_conv = scale_inv * (grad_unit - mean_one - unit_field * mean_two)
    grad_bias = jnp.sum(grad_conv, axis=(0, 1, 2))
    tap_sums = []
    for tap_row in range(7):
        for tap_col in range(7):
            window = padded[:, tap_row : tap_row + map_side, tap_col : tap_col + map_side, :]
            tap_sums.append(jnp.sum(window * grad_conv, axis=(0, 1, 2)))
    grad_kernel = jnp.stack(tap_sums).reshape(7, 7, unit_field.shape[-1])
    return (grad_kernel, jnp.stack([grad_bias, grad_gain, grad_shift]))


def exchange_sum(values, axes):
    count = lax.axis_size(axes)
    return lax.all_to_all(values.reshape(count, -1), axes, 0, 0, tiled=True).sum(0)


def exchange_gather(values, axes):
    count = lax.axis_size(axes)
    copies = jnp.broadcast_to(values[None], (count,) + values.shape)
    return lax.all_to_all(copies, axes, 0, 0, tiled=True).reshape(-1)


def packed_sum(values):
    inner, outer = ("dp_hi", "row") + FSDP, "z"
    values = exchange_sum(values, inner)
    values = exchange_gather(values, outer).reshape(lax.axis_size(outer), -1).sum(0)
    return exchange_gather(values, inner)


DP = ("dp_hi", "z")
FSDP = ("y", "core")


def shards(images, kernel, conv_bias, ln_gain, ln_shift, w_up, cotangent):
    full_maps = lax.all_gather(images, "row", axis=1, tiled=True)
    padded, unit_field, scale_inv, normed = conv_norm(
        full_maps, kernel, conv_bias, ln_gain, ln_shift
    )
    channels = normed.shape[-1]
    hidden_units = w_up.shape[1]
    flat = normed.reshape(-1, channels)
    weights = lax.all_gather(w_up, FSDP, axis=0, tiled=True)
    pre_act = jnp.dot(flat, weights, preferred_element_type=jnp.float32)
    activated, pullback = jax.vjp(gelu_exact, pre_act)
    hidden = activated.astype(jnp.bfloat16)
    grad_pre = pullback(cotangent.reshape(-1, hidden_units).astype(jnp.float32))[0].astype(
        jnp.bfloat16
    )
    grad_weight = lax.psum_scatter(
        lax.dot_general(
            flat, grad_pre, (((0,), (0,)), ((), ())), preferred_element_type=jnp.float32
        ).astype(jnp.bfloat16),
        FSDP,
        scatter_dimension=0,
        tiled=True,
    ).astype(jnp.float32)
    grad_normed = lax.dot_general(
        grad_pre, weights, (((1,), (1,)), ((), ())), preferred_element_type=jnp.float32
    )
    kernel_part, vector_part = norm_conv_grads(
        padded, unit_field, scale_inv, grad_normed.reshape(unit_field.shape), ln_gain
    )
    taps = kernel_part.shape[0] * kernel_part.shape[1]
    packed = jnp.concatenate([kernel_part.reshape(taps, channels), vector_part], axis=0)
    packed = packed_sum(packed.reshape(-1)).reshape(packed.shape)
    grad_kernel = packed[:taps].reshape(kernel_part.shape)
    grad_vectors = packed[taps:]
    return (hidden.reshape(cotangent.shape), grad_weight[None], grad_kernel, grad_vectors)


def solution(mesh):
    replicas, rows, fsdp = (mesh.shape[name] for name in ("dp", "row", "fsdp"))
    fine = jax.sharding.Mesh(
        mesh.devices.reshape(2, replicas // 2, rows, fsdp // 2, 2), ("dp_hi", "z", "row") + FSDP
    )
    return jax.shard_map(
        shards,
        mesh=fine,
        in_specs=(
            P(DP + FSDP, "row", None, None),
            P(),
            P(),
            P(),
            P(),
            P(FSDP, "row"),
            P(DP + FSDP, None, None, "row"),
        ),
        out_specs=(P(DP + FSDP, None, None, "row"), P(DP, FSDP, "row"), P(), P()),
        check_vma=False,
    )
```

```python
import jax
import jax.numpy as jnp
from jax import lax
from jax.sharding import PartitionSpec as P

norm_epsilon = 1e-06


def gelu_exact(values):
    return jax.nn.gelu(values, approximate=False)


def conv_norm(images, kernel, conv_bias, ln_gain, ln_shift):
    source = images.astype(jnp.float32)
    map_side = source.shape[1]
    padded = jnp.pad(source, ((0, 0), (3, 3), (3, 3), (0, 0)))
    conv_out = jnp.zeros_like(source) + conv_bias
    for tap_row in range(7):
        for tap_col in range(7):
            conv_out = (
                conv_out
                + padded[:, tap_row : tap_row + map_side, tap_col : tap_col + map_side, :]
                * kernel[tap_row, tap_col]
            )
    centre = jnp.mean(conv_out, axis=-1, keepdims=True)
    spread = jnp.mean(jnp.square(conv_out - centre), axis=-1, keepdims=True)
    scale_inv = lax.rsqrt(spread + norm_epsilon)
    unit_field = (conv_out - centre) * scale_inv
    normed = (unit_field * ln_gain + ln_shift).astype(jnp.bfloat16)
    return (padded, unit_field, scale_inv, normed)


def norm_conv_grads(padded, unit_field, scale_inv, grad_normed, ln_gain):
    map_side = unit_field.shape[1]
    grad_gain = jnp.sum(grad_normed * unit_field, axis=(0, 1, 2))
    grad_shift = jnp.sum(grad_normed, axis=(0, 1, 2))
    grad_unit = grad_normed * ln_gain
    mean_one = jnp.mean(grad_unit, axis=-1, keepdims=True)
    mean_two = jnp.mean(grad_unit * unit_field, axis=-1, keepdims=True)
    grad_conv = scale_inv * (grad_unit - mean_one - unit_field * mean_two)
    grad_bias = jnp.sum(grad_conv, axis=(0, 1, 2))
    tap_sums = []
    for tap_row in range(7):
        for tap_col in range(7):
            window = padded[:, tap_row : tap_row + map_side, tap_col : tap_col + map_side, :]
            tap_sums.append(jnp.sum(window * grad_conv, axis=(0, 1, 2)))
    grad_kernel = jnp.stack(tap_sums).reshape(7, 7, unit_field.shape[-1])
    return (grad_kernel, jnp.stack([grad_bias, grad_gain, grad_shift]))


def exchange_sum(values, axes):
    count = lax.axis_size(axes)
    return lax.all_to_all(values.reshape(count, -1), axes, 0, 0, tiled=True).sum(0)


def exchange_gather(values, axes):
    count = lax.axis_size(axes)
    copies = jnp.broadcast_to(values[None], (count,) + values.shape)
    return lax.all_to_all(copies, axes, 0, 0, tiled=True).reshape(-1)


def packed_sum(values):
    inner, outer = ("dp_hi", "row") + FSDP, "z"
    values = exchange_sum(values, inner)
    values = exchange_gather(values, outer).reshape(lax.axis_size(outer), -1).sum(0)
    return exchange_gather(values, inner)


DP = ("dp_hi", "z")
FSDP = ("y", "core")


def shards(images, kernel, conv_bias, ln_gain, ln_shift, w_up, cotangent):
    rows = lax.axis_size("row")
    others = lax.ppermute(images, "row", [(i, (i + 1) % rows) for i in range(rows)])
    first = lax.axis_index("row") == 0
    full_maps = jnp.where(
        first,
        jnp.concatenate([images, others], axis=1),
        jnp.concatenate([others, images], axis=1),
    )
    padded, unit_field, scale_inv, normed = conv_norm(
        full_maps, kernel, conv_bias, ln_gain, ln_shift
    )
    channels = normed.shape[-1]
    hidden_units = w_up.shape[1]
    flat = normed.reshape(-1, channels)
    weights = lax.all_gather(w_up, FSDP, axis=0, tiled=True)
    pre_act = jnp.dot(flat, weights, preferred_element_type=jnp.float32)
    activated, pullback = jax.vjp(gelu_exact, pre_act)
    hidden = activated.astype(jnp.bfloat16)
    grad_pre = pullback(cotangent.reshape(-1, hidden_units).astype(jnp.float32))[0].astype(
        jnp.bfloat16
    )
    grad_weight = lax.psum_scatter(
        lax.dot_general(
            flat, grad_pre, (((0,), (0,)), ((), ())), preferred_element_type=jnp.float32
        ).astype(jnp.bfloat16),
        FSDP,
        scatter_dimension=0,
        tiled=True,
    ).astype(jnp.float32)
    grad_normed = lax.dot_general(
        grad_pre, weights, (((1,), (1,)), ((), ())), preferred_element_type=jnp.float32
    )
    kernel_part, vector_part = norm_conv_grads(
        padded, unit_field, scale_inv, grad_normed.reshape(unit_field.shape), ln_gain
    )
    taps = kernel_part.shape[0] * kernel_part.shape[1]
    packed = jnp.concatenate([kernel_part.reshape(taps, channels), vector_part], axis=0)
    packed = packed_sum(packed.reshape(-1)).reshape(packed.shape)
    grad_kernel = packed[:taps].reshape(kernel_part.shape)
    grad_vectors = packed[taps:]
    return (hidden.reshape(cotangent.shape), grad_weight[None], grad_kernel, grad_vectors)


def solution(mesh):
    replicas, rows, fsdp = (mesh.shape[name] for name in ("dp", "row", "fsdp"))
    fine = jax.sharding.Mesh(
        mesh.devices.reshape(2, replicas // 2, rows, fsdp // 2, 2), ("dp_hi", "z", "row") + FSDP
    )
    return jax.shard_map(
        shards,
        mesh=fine,
        in_specs=(
            P(DP + FSDP, "row", None, None),
            P(),
            P(),
            P(),
            P(),
            P(FSDP, "row"),
            P(DP + FSDP, None, None, "row"),
        ),
        out_specs=(P(DP + FSDP, None, None, "row"), P(DP, FSDP, "row"), P(), P()),
        check_vma=False,
    )
```

```python
import jax
import jax.numpy as jnp
from jax import lax
from jax.sharding import PartitionSpec as P

norm_epsilon = 1e-06


def gelu_exact(values):
    return jax.nn.gelu(values, approximate=False)


def conv_norm(images, kernel, conv_bias, ln_gain, ln_shift):
    source = images.astype(jnp.float32)
    map_side = source.shape[1]
    padded = jnp.pad(source, ((0, 0), (3, 3), (3, 3), (0, 0)))
    conv_out = jnp.zeros_like(source) + conv_bias
    for tap_row in range(7):
        for tap_col in range(7):
            conv_out = (
                conv_out
                + padded[:, tap_row : tap_row + map_side, tap_col : tap_col + map_side, :]
                * kernel[tap_row, tap_col]
            )
    centre = jnp.mean(conv_out, axis=-1, keepdims=True)
    spread = jnp.mean(jnp.square(conv_out - centre), axis=-1, keepdims=True)
    scale_inv = lax.rsqrt(spread + norm_epsilon)
    unit_field = (conv_out - centre) * scale_inv
    normed = (unit_field * ln_gain + ln_shift).astype(jnp.bfloat16)
    return (padded, unit_field, scale_inv, normed)


def norm_conv_grads(padded, unit_field, scale_inv, grad_normed, ln_gain):
    map_side = unit_field.shape[1]
    grad_gain = jnp.sum(grad_normed * unit_field, axis=(0, 1, 2))
    grad_shift = jnp.sum(grad_normed, axis=(0, 1, 2))
    grad_unit = grad_normed * ln_gain
    mean_one = jnp.mean(grad_unit, axis=-1, keepdims=True)
    mean_two = jnp.mean(grad_unit * unit_field, axis=-1, keepdims=True)
    grad_conv = scale_inv * (grad_unit - mean_one - unit_field * mean_two)
    grad_bias = jnp.sum(grad_conv, axis=(0, 1, 2))
    tap_sums = []
    for tap_row in range(7):
        for tap_col in range(7):
            window = padded[:, tap_row : tap_row + map_side, tap_col : tap_col + map_side, :]
            tap_sums.append(jnp.sum(window * grad_conv, axis=(0, 1, 2)))
    grad_kernel = jnp.stack(tap_sums).reshape(7, 7, unit_field.shape[-1])
    return (grad_kernel, jnp.stack([grad_bias, grad_gain, grad_shift]))


def exchange_sum(values, axes):
    count = lax.axis_size(axes)
    return lax.all_to_all(values.reshape(count, -1), axes, 0, 0, tiled=True).sum(0)


def exchange_gather(values, axes):
    count = lax.axis_size(axes)
    copies = jnp.broadcast_to(values[None], (count,) + values.shape)
    return lax.all_to_all(copies, axes, 0, 0, tiled=True).reshape(-1)


def packed_sum(values):
    inner, outer = ("dp_hi", "row") + FSDP, "z"
    values = exchange_sum(values, inner)
    values = exchange_gather(values, outer).reshape(lax.axis_size(outer), -1).sum(0)
    return exchange_gather(values, inner)


DP = ("dp_hi", "z")
FSDP = ("y", "core")


def shards(images, kernel, conv_bias, ln_gain, ln_shift, w_up, cotangent):
    full_maps = lax.all_gather(images, "row", axis=1, tiled=True)
    padded, unit_field, scale_inv, normed = conv_norm(
        full_maps, kernel, conv_bias, ln_gain, ln_shift
    )
    channels = normed.shape[-1]
    hidden_units = w_up.shape[1]
    flat = normed.reshape(-1, channels)
    weights = lax.all_gather(w_up, FSDP, axis=0, tiled=True)
    pre_act = jnp.dot(flat, weights, preferred_element_type=jnp.float32)
    activated, pullback = jax.vjp(gelu_exact, pre_act)
    hidden = activated.astype(jnp.bfloat16)
    grad_pre = pullback(cotangent.reshape(-1, hidden_units).astype(jnp.float32))[0].astype(
        jnp.bfloat16
    )
    grad_weight = lax.psum_scatter(
        lax.dot_general(
            flat, grad_pre, (((0,), (0,)), ((), ())), preferred_element_type=jnp.float32
        ).astype(jnp.bfloat16),
        FSDP,
        scatter_dimension=0,
        tiled=True,
    ).astype(jnp.float32)
    grad_normed = lax.dot_general(
        grad_pre, weights, (((1,), (1,)), ((), ())), preferred_element_type=jnp.float32
    )
    kernel_part, vector_part = norm_conv_grads(
        padded, unit_field, scale_inv, grad_normed.reshape(unit_field.shape), ln_gain
    )
    taps = kernel_part.shape[0] * kernel_part.shape[1]
    shards_of = lax.axis_size(("dp_hi", "row") + FSDP)
    spare = -(taps + vector_part.shape[0]) % shards_of
    padding = jnp.zeros((spare, channels), jnp.float32)
    packed = jnp.concatenate([kernel_part.reshape(taps, channels), vector_part, padding], axis=0)
    packed = packed_sum(packed.reshape(-1)).reshape(packed.shape)
    grad_kernel = packed[:taps].reshape(kernel_part.shape)
    grad_vectors = packed[taps : taps + vector_part.shape[0]]
    return (hidden.reshape(cotangent.shape), grad_weight[None], grad_kernel, grad_vectors)


def solution(mesh):
    replicas, rows, fsdp = (mesh.shape[name] for name in ("dp", "row", "fsdp"))
    fine = jax.sharding.Mesh(
        mesh.devices.reshape(2, replicas // 2, rows, fsdp // 2, 2), ("dp_hi", "z", "row") + FSDP
    )
    return jax.shard_map(
        shards,
        mesh=fine,
        in_specs=(
            P(DP + FSDP, "row", None, None),
            P(),
            P(),
            P(),
            P(),
            P(FSDP, "row"),
            P(DP + FSDP, None, None, "row"),
        ),
        out_specs=(P(DP + FSDP, None, None, "row"), P(DP, FSDP, "row"), P(), P()),
        check_vma=False,
    )
```

```python
import jax
import jax.numpy as jnp
from jax import lax
from jax.sharding import PartitionSpec as P

norm_epsilon = 1e-06


def gelu_exact(values):
    return jax.nn.gelu(values, approximate=False)


def conv_norm(images, kernel, conv_bias, ln_gain, ln_shift):
    source = images.astype(jnp.float32)
    map_side = source.shape[1]
    padded = jnp.pad(source, ((0, 0), (3, 3), (3, 3), (0, 0)))
    conv_out = jnp.zeros_like(source) + conv_bias
    for tap_row in range(7):
        for tap_col in range(7):
            conv_out = (
                conv_out
                + padded[:, tap_row : tap_row + map_side, tap_col : tap_col + map_side, :]
                * kernel[tap_row, tap_col]
            )
    centre = jnp.mean(conv_out, axis=-1, keepdims=True)
    spread = jnp.mean(jnp.square(conv_out - centre), axis=-1, keepdims=True)
    scale_inv = lax.rsqrt(spread + norm_epsilon)
    unit_field = (conv_out - centre) * scale_inv
    normed = (unit_field * ln_gain + ln_shift).astype(jnp.bfloat16)
    return (padded, unit_field, scale_inv, normed)


def norm_conv_grads(padded, unit_field, scale_inv, grad_normed, ln_gain):
    map_side = unit_field.shape[1]
    grad_gain = jnp.sum(grad_normed * unit_field, axis=(0, 1, 2))
    grad_shift = jnp.sum(grad_normed, axis=(0, 1, 2))
    grad_unit = grad_normed * ln_gain
    mean_one = jnp.mean(grad_unit, axis=-1, keepdims=True)
    mean_two = jnp.mean(grad_unit * unit_field, axis=-1, keepdims=True)
    grad_conv = scale_inv * (grad_unit - mean_one - unit_field * mean_two)
    grad_bias = jnp.sum(grad_conv, axis=(0, 1, 2))
    tap_sums = []
    for tap_row in range(7):
        for tap_col in range(7):
            window = padded[:, tap_row : tap_row + map_side, tap_col : tap_col + map_side, :]
            tap_sums.append(jnp.sum(window * grad_conv, axis=(0, 1, 2)))
    grad_kernel = jnp.stack(tap_sums).reshape(7, 7, unit_field.shape[-1])
    return (grad_kernel, jnp.stack([grad_bias, grad_gain, grad_shift]))


def exchange_sum(values, axes):
    count = lax.axis_size(axes)
    return lax.all_to_all(values.reshape(count, -1), axes, 0, 0, tiled=True).sum(0)


def exchange_gather(values, axes):
    count = lax.axis_size(axes)
    copies = jnp.broadcast_to(values[None], (count,) + values.shape)
    return lax.all_to_all(copies, axes, 0, 0, tiled=True).reshape(-1)


def packed_sum(values):
    cores = lax.axis_size("core")
    bit = lax.axis_index("core") % 2
    swap = [(i, i ^ 1) for i in range(cores)]
    half = values.shape[0] // 2
    keep = lax.dynamic_slice_in_dim(values, bit * half, half)
    send = lax.dynamic_slice_in_dim(values, (1 - bit) * half, half)
    values = keep + lax.ppermute(send, "core", swap)
    inner, outer = ("dp_hi", "row", "y"), "z"
    values = exchange_sum(values, inner)
    values = exchange_gather(values, outer).reshape(lax.axis_size(outer), -1).sum(0)
    values = exchange_gather(values, inner)
    other = lax.ppermute(values, "core", swap)
    return jnp.where(bit == 0, jnp.concatenate([values, other]), jnp.concatenate([other, values]))


DP = ("dp_hi", "z")
FSDP = ("y", "core")


def shards(images, kernel, conv_bias, ln_gain, ln_shift, w_up, cotangent):
    full_maps = lax.all_gather(images, "row", axis=1, tiled=True)
    padded, unit_field, scale_inv, normed = conv_norm(
        full_maps, kernel, conv_bias, ln_gain, ln_shift
    )
    channels = normed.shape[-1]
    hidden_units = w_up.shape[1]
    flat = normed.reshape(-1, channels)
    weights = lax.all_gather(w_up, FSDP, axis=0, tiled=True)
    pre_act = jnp.dot(flat, weights, preferred_element_type=jnp.float32)
    activated, pullback = jax.vjp(gelu_exact, pre_act)
    hidden = activated.astype(jnp.bfloat16)
    grad_pre = pullback(cotangent.reshape(-1, hidden_units).astype(jnp.float32))[0].astype(
        jnp.bfloat16
    )
    grad_weight = lax.psum_scatter(
        lax.dot_general(
            flat, grad_pre, (((0,), (0,)), ((), ())), preferred_element_type=jnp.float32
        ).astype(jnp.bfloat16),
        FSDP,
        scatter_dimension=0,
        tiled=True,
    ).astype(jnp.float32)
    grad_normed = lax.dot_general(
        grad_pre, weights, (((1,), (1,)), ((), ())), preferred_element_type=jnp.float32
    )
    kernel_part, vector_part = norm_conv_grads(
        padded, unit_field, scale_inv, grad_normed.reshape(unit_field.shape), ln_gain
    )
    taps = kernel_part.shape[0] * kernel_part.shape[1]
    packed = jnp.concatenate([kernel_part.reshape(taps, channels), vector_part], axis=0)
    packed = packed_sum(packed.reshape(-1)).reshape(packed.shape)
    grad_kernel = packed[:taps].reshape(kernel_part.shape)
    grad_vectors = packed[taps:]
    return (hidden.reshape(cotangent.shape), grad_weight[None], grad_kernel, grad_vectors)


def solution(mesh):
    replicas, rows, fsdp = (mesh.shape[name] for name in ("dp", "row", "fsdp"))
    fine = jax.sharding.Mesh(
        mesh.devices.reshape(2, replicas // 2, rows, fsdp // 2, 2), ("dp_hi", "z", "row") + FSDP
    )
    return jax.shard_map(
        shards,
        mesh=fine,
        in_specs=(
            P(DP + FSDP, "row", None, None),
            P(),
            P(),
            P(),
            P(),
            P(FSDP, "row"),
            P(DP + FSDP, None, None, "row"),
        ),
        out_specs=(P(DP + FSDP, None, None, "row"), P(DP, FSDP, "row"), P(), P()),
        check_vma=False,
    )
```

```python
import jax
import jax.numpy as jnp
from jax import lax
from jax.sharding import PartitionSpec as P

norm_epsilon = 1e-06


def gelu_exact(values):
    return jax.nn.gelu(values, approximate=False)


def conv_norm(images, kernel, conv_bias, ln_gain, ln_shift):
    source = images.astype(jnp.float32)
    map_side = source.shape[1]
    padded = jnp.pad(source, ((0, 0), (3, 3), (3, 3), (0, 0)))
    conv_out = jnp.zeros_like(source) + conv_bias
    for tap_row in range(7):
        for tap_col in range(7):
            conv_out = (
                conv_out
                + padded[:, tap_row : tap_row + map_side, tap_col : tap_col + map_side, :]
                * kernel[tap_row, tap_col]
            )
    centre = jnp.mean(conv_out, axis=-1, keepdims=True)
    spread = jnp.mean(jnp.square(conv_out - centre), axis=-1, keepdims=True)
    scale_inv = lax.rsqrt(spread + norm_epsilon)
    unit_field = (conv_out - centre) * scale_inv
    normed = (unit_field * ln_gain + ln_shift).astype(jnp.bfloat16)
    return (padded, unit_field, scale_inv, normed)


def norm_conv_grads(padded, unit_field, scale_inv, grad_normed, ln_gain):
    map_side = unit_field.shape[1]
    grad_gain = jnp.sum(grad_normed * unit_field, axis=(0, 1, 2))
    grad_shift = jnp.sum(grad_normed, axis=(0, 1, 2))
    grad_unit = grad_normed * ln_gain
    mean_one = jnp.mean(grad_unit, axis=-1, keepdims=True)
    mean_two = jnp.mean(grad_unit * unit_field, axis=-1, keepdims=True)
    grad_conv = scale_inv * (grad_unit - mean_one - unit_field * mean_two)
    grad_bias = jnp.sum(grad_conv, axis=(0, 1, 2))
    tap_sums = []
    for tap_row in range(7):
        for tap_col in range(7):
            window = padded[:, tap_row : tap_row + map_side, tap_col : tap_col + map_side, :]
            tap_sums.append(jnp.sum(window * grad_conv, axis=(0, 1, 2)))
    grad_kernel = jnp.stack(tap_sums).reshape(7, 7, unit_field.shape[-1])
    return (grad_kernel, jnp.stack([grad_bias, grad_gain, grad_shift]))


def exchange_sum(values, axes):
    count = lax.axis_size(axes)
    return lax.all_to_all(values.reshape(count, -1), axes, 0, 0, tiled=True).sum(0)


def exchange_gather(values, axes):
    count = lax.axis_size(axes)
    copies = jnp.broadcast_to(values[None], (count,) + values.shape)
    return lax.all_to_all(copies, axes, 0, 0, tiled=True).reshape(-1)


def packed_sum(values):
    inner, outer = ("dp_hi", "z", "row", "core"), "y"
    values = exchange_sum(values, inner)
    values = exchange_gather(values, outer).reshape(lax.axis_size(outer), -1).sum(0)
    return exchange_gather(values, inner)


DP = ("dp_hi", "z")
FSDP = ("y", "core")


def shards(images, kernel, conv_bias, ln_gain, ln_shift, w_up, cotangent):
    full_maps = lax.all_gather(images, "row", axis=1, tiled=True)
    padded, unit_field, scale_inv, normed = conv_norm(
        full_maps, kernel, conv_bias, ln_gain, ln_shift
    )
    channels = normed.shape[-1]
    hidden_units = w_up.shape[1]
    flat = normed.reshape(-1, channels)
    weights = lax.all_gather(w_up, FSDP, axis=0, tiled=True)
    pre_act = jnp.dot(flat, weights, preferred_element_type=jnp.float32)
    activated, pullback = jax.vjp(gelu_exact, pre_act)
    hidden = activated.astype(jnp.bfloat16)
    grad_pre = pullback(cotangent.reshape(-1, hidden_units).astype(jnp.float32))[0].astype(
        jnp.bfloat16
    )
    grad_weight = lax.psum_scatter(
        lax.dot_general(
            flat, grad_pre, (((0,), (0,)), ((), ())), preferred_element_type=jnp.float32
        ).astype(jnp.bfloat16),
        FSDP,
        scatter_dimension=0,
        tiled=True,
    ).astype(jnp.float32)
    grad_normed = lax.dot_general(
        grad_pre, weights, (((1,), (1,)), ((), ())), preferred_element_type=jnp.float32
    )
    kernel_part, vector_part = norm_conv_grads(
        padded, unit_field, scale_inv, grad_normed.reshape(unit_field.shape), ln_gain
    )
    taps = kernel_part.shape[0] * kernel_part.shape[1]
    packed = jnp.concatenate([kernel_part.reshape(taps, channels), vector_part], axis=0)
    packed = packed_sum(packed.reshape(-1)).reshape(packed.shape)
    grad_kernel = packed[:taps].reshape(kernel_part.shape)
    grad_vectors = packed[taps:]
    return (hidden.reshape(cotangent.shape), grad_weight[None], grad_kernel, grad_vectors)


def solution(mesh):
    replicas, rows, fsdp = (mesh.shape[name] for name in ("dp", "row", "fsdp"))
    fine = jax.sharding.Mesh(
        mesh.devices.reshape(2, replicas // 2, rows, fsdp // 2, 2), ("dp_hi", "z", "row") + FSDP
    )
    return jax.shard_map(
        shards,
        mesh=fine,
        in_specs=(
            P(DP + FSDP, "row", None, None),
            P(),
            P(),
            P(),
            P(),
            P(FSDP, "row"),
            P(DP + FSDP, None, None, "row"),
        ),
        out_specs=(P(DP + FSDP, None, None, "row"), P(DP, FSDP, "row"), P(), P()),
        check_vma=False,
    )
```
